32 devices in a mesh: well: 4 (over y, x), tile: 8 (over z, core).
Axes of the slice: x: 2, y: 2, z: 4, core: 2. Of those that a mesh axis runs over, the one named last changes fastest.
Arguments:
- prior_state: float32 [3, 200, 8192], P(None, None, 'tile'), may hold values from -6 to 6
- pred_data: float32 [4096, 200], P(('well', 'tile')), may hold values from -6 to 6
- obs_pert: float32 [4096, 200], P(('well', 'tile')), may hold values from -12 to 12
- obs_std: float32 [4096], P(('well', 'tile')), may hold values from 0.5 to 2
- loc_mask: int32 [8, 32], P('tile', 'well'), may hold values from 0 to 1, as said below
- taper_level: int32 [8, 32], P('tile', 'well'), may hold values from 1 to 4
Outputs:
- analysis: float32 [3, 200, 8192], P(None, 'well', 'tile')
The draws below stay inside these ranges and needn't reach their ends.
Inputs may be any that keep to these rules, and one draw needn't show every extreme that they name: `loc_mask`: each tile is localized to a set of data blocks whose size varies strongly from tile to tile; some tile is localized to most blocks.
All inputs are finite; a program needn't handle non-finite values.
Results may differ from the reference program's by a relative error of at most 0.0003.
Values sent between devices are 32-bit elements; how exact they have to be, the bound alone decides.
No kernel may reach another device: no remote copies, remote signals or barrier semaphores. Data moves between devices by JAX's collectives and lax.ppermute only.
A program may use at most 64 MiB of HBM per device.

```python
import math
import jax
import jax.numpy as jnp
from jax import lax

MEMBERS = 200
VARS = 3
BLOCK = 128
NBLK = 32
CELL_DEV = 1024
DATA = 4096
TILES = 8
CELLS = 8192


def draw_loc_mask(key, part):
    key_rank, key_heavy, key_pick, key_light, key_full = jax.random.split(key, 5)
    scores = jax.random.randint(key_rank, (TILES, NBLK), 0, 1 << 20) * NBLK + jnp.arange(NBLK, dtype=jnp.int32)[None, :]
    ranks = jnp.argsort(jnp.argsort(scores, axis=1), axis=1)
    heavy = jax.random.randint(key_heavy, (TILES,), 0, 4) == 0
    chosen = jax.random.randint(key_pick, (), 0, TILES)
    heavy = jnp.logical_or(heavy, jnp.arange(TILES, dtype=jnp.int32) == chosen)
    light_count = jax.random.randint(key_light, (TILES,), 1, max(NBLK * 3 // 8, 2))
    heavy_count = jax.random.randint(key_full, (TILES,), NBLK * 3 // 4, NBLK + 1)
    counts = jnp.where(heavy, heavy_count, light_count)
    return (ranks < counts[:, None]).astype(jnp.int32)


def plant(drawn, key, smallest, largest):
    dims = drawn.shape
    spot = [jax.random.randint(jax.random.fold_in(key, axis), (), 0, dims[axis]) for axis in range(len(dims))]
    drawn = drawn.at[tuple(spot)].set(smallest)
    longest = dims.index(max(dims))
    spot[longest] = (spot[longest] + 1) % dims[longest]
    return drawn.at[tuple(spot)].set(largest)


def steps_of(stream_key, extent, shards, smallest, top_value):
    loudness = 1.0
    for dim, blocks in shards:
        draws = jax.random.uniform(jax.random.fold_in(jax.random.fold_in(stream_key, 6), dim), (blocks,), jnp.float32, smallest / len(shards), top_value / len(shards))
        loudness = loudness * jnp.repeat(jnp.exp(draws), extent[dim] // blocks).reshape((-1,) + (1,) * (len(extent) - 1 - dim))
    return loudness


def gaussian(rng, dims, deviation, bound, shards=(), held_as=jnp.bfloat16):
    drawn = jax.random.normal(rng, dims, jnp.float32) * deviation
    if len(shards) > 0:
        drawn = steps_of(rng, dims, shards, -0.22, 0.18) * drawn
    return jnp.clip(drawn, min=-bound, max=bound).astype(held_as)


def setup_inputs(seed: int = 0) -> dict:
    streams_of = jax.random.split(jax.random.key(seed), 7)
    return {
        "prior_state": gaussian(streams_of[0], (VARS, MEMBERS, CELLS), 1.0, 6.0, ((2, 8),), jnp.float32),
        "pred_data": gaussian(streams_of[1], (DATA, MEMBERS), 1.0, 6.0, ((0, 32),), jnp.float32),
        "obs_pert": gaussian(streams_of[2], (DATA, MEMBERS), 2.0, 12.0, ((0, 32),), jnp.float32),
        "obs_std": jnp.clip(jnp.exp(math.log(2.0) - 1.3862944 * jax.random.uniform(streams_of[3], (DATA,), jnp.float32) ** steps_of(streams_of[3], (DATA,), ((0, 32),), -0.2, 0.2)), 0.5, 2.0),
        "loc_mask": draw_loc_mask(jax.random.fold_in(streams_of[6], 71), 0),
        "taper_level": plant(jax.random.randint(streams_of[5], (TILES, NBLK), 1, 5), jax.random.fold_in(streams_of[5], 1), 1, 4).astype(jnp.int32),
    }


def chol_apply(system, right):
    factor = jnp.linalg.cholesky(system)
    middle = lax.linalg.triangular_solve(factor, right, left_side=True, lower=True, transpose_a=False)
    return lax.linalg.triangular_solve(factor, middle, left_side=True, lower=True, transpose_a=True)

def reference(prior_state, pred_data, obs_pert, obs_std, loc_mask, taper_level):
    highest = lax.Precision.HIGHEST
    members = pred_data.shape[1]
    norm_factor = 1.0 / jnp.sqrt(jnp.float32(members - 1))
    data_anom = (pred_data - lax.optimization_barrier(jnp.mean(pred_data, axis=1, keepdims=True))) * norm_factor
    innov = obs_pert - pred_data
    row_weight = 1.0 / (4.0 * obs_std * obs_std)
    scaled = row_weight[:, None] * data_anom
    gram_matrix = jnp.dot(data_anom.T, scaled, precision=highest)
    cross_matrix = jnp.dot(scaled.T, innov, precision=highest)
    system = jnp.eye(members, dtype=jnp.float32) + gram_matrix
    solved = chol_apply(system, cross_matrix)
    gain_rows = row_weight[:, None] * innov - jnp.dot(scaled, solved, precision=highest)
    block_space = jnp.einsum('kbn,kbm->knm', data_anom.reshape(NBLK, BLOCK, members), gain_rows.reshape(NBLK, BLOCK, members), precision=highest)
    taper = loc_mask.astype(jnp.float32) * taper_level.astype(jnp.float32) / 4.0
    state_anom = (prior_state - lax.optimization_barrier(jnp.mean(prior_state, axis=1, keepdims=True))) * norm_factor
    tiled = state_anom.reshape(VARS, members, TILES, CELL_DEV).transpose(2, 0, 1, 3)

    def per_tile(pair):
        anom_tile, taper_row = pair
        space = jnp.einsum('k,knm->nm', taper_row, block_space, precision=highest)
        return jnp.einsum('vnc,nm->vmc', anom_tile, space, precision=highest)
    increment = lax.map(per_tile, (tiled, taper))
    increment = increment.transpose(1, 2, 0, 3).reshape(VARS, members, TILES * CELL_DEV)
    return prior_state + increment
```

```python
import jax
import jax.numpy as jnp
from jax import lax
from jax.sharding import PartitionSpec as P

BLOCK = 128


def chol_apply(system, right):
    factor = jnp.linalg.cholesky(system)
    middle = lax.linalg.triangular_solve(
        factor, right, left_side=True, lower=True, transpose_a=False
    )
    return lax.linalg.triangular_solve(factor, middle, left_side=True, lower=True, transpose_a=True)


def prepare(pred_rows, obs_rows, std_rows, norm_factor):
    data_anom = (pred_rows - jnp.mean(pred_rows, axis=1, keepdims=True)) * norm_factor
    innov = obs_rows - pred_rows
    row_weight = 1.0 / (4.0 * std_rows * std_rows)
    scaled = row_weight[:, None] * data_anom
    return (data_anom, innov, row_weight, scaled)


def bit_of(axis, k):
    return (lax.axis_index(axis) // k) % 2


def swap(x, axis, k):
    size = lax.axis_size(axis)
    return lax.ppermute(x, axis, [(i, i ^ k) for i in range(size)])


def axis_bits(axis):
    size = lax.axis_size(axis)
    out, k = [], 1
    while k < size:
        out.append((axis, k))
        k *= 2
    return out


def all_sum(x, steps):
    halved = []
    for axis, k in steps:
        rows = x.shape[0]
        if rows % 2 == 0:
            half = rows // 2
            hi = bit_of(axis, k) == 1
            keep = jnp.where(hi, x[half:], x[:half])
            send = jnp.where(hi, x[:half], x[half:])
            x = keep + swap(send, axis, k)
            halved.append((axis, k))
        else:
            x = x + swap(x, axis, k)
    for axis, k in reversed(halved):
        other = swap(x, axis, k)
        hi = bit_of(axis, k) == 1
        x = jnp.where(hi, jnp.concatenate([other, x], 0), jnp.concatenate([x, other], 0))
    return x


def well_reduce(full, split):
    for axis, k in reversed(axis_bits("well")):
        rows = split.shape[0]
        half = rows // 2
        hi = bit_of(axis, k) == 1
        keep = jnp.where(hi, split[half:], split[:half])
        send = jnp.where(hi, split[:half], split[half:])
        got = swap(jnp.concatenate([full, send], 0), axis, k)
        full = full + got[: full.shape[0]]
        split = keep + got[full.shape[0]:]
    return full, split


def shards(prior_state, pred_data, obs_pert, obs_std, loc_mask, taper_level):
    highest = lax.Precision.HIGHEST
    members = pred_data.shape[1]
    norm_factor = 1.0 / jnp.sqrt(jnp.float32(members - 1))
    data_anom, innov, row_weight, scaled = prepare(pred_data, obs_pert, obs_std, norm_factor)

    stacked = jnp.concatenate(
        [
            jnp.dot(data_anom.T, scaled, precision=highest),
            jnp.dot(scaled.T, innov, precision=highest),
        ],
        0,
    )
    order = axis_bits("tile")[:1] + axis_bits("well") + axis_bits("tile")[1:]
    stacked = all_sum(stacked, order)
    gram_matrix, cross_matrix = stacked[:members], stacked[members:]
    own_count = members // lax.axis_size("well")
    own_start = lax.axis_index("well") * own_count
    cross_mine = lax.dynamic_slice_in_dim(cross_matrix, own_start, own_count, 1)
    system = jnp.eye(members, dtype=jnp.float32) + gram_matrix
    solved_mine = chol_apply(system, cross_mine)

    packed = jnp.concatenate([data_anom, innov, row_weight[:, None]], 1)
    group = lax.all_gather(packed, "tile", axis=0, tiled=True)
    group_anom, group_innov, group_weight = (
        group[:, :members],
        group[:, members : 2 * members],
        group[:, 2 * members],
    )
    taper_row = loc_mask[0].astype(jnp.float32) * taper_level[0].astype(jnp.float32) / 4.0
    row_taper = jnp.repeat(taper_row, BLOCK)
    tapered = (row_taper * group_weight)[:, None] * group_anom
    both = lax.dot_general(
        jnp.concatenate([group_anom, group_innov], 1),
        tapered,
        (((0,), (0,)), ((), ())),
        precision=highest,
    )
    taper_gram, taper_cross_t = both[:members], both[members:]
    taper_gram, cross_t_mine = well_reduce(taper_gram, taper_cross_t)

    space_t = cross_t_mine - lax.dot_general(
        solved_mine, taper_gram, (((0,), (1,)), ((), ())), precision=highest
    )
    state_anom = (prior_state - jnp.mean(prior_state, axis=1, keepdims=True)) * norm_factor
    increment = jnp.einsum("vnc,mn->vmc", state_anom, space_t, precision=highest)
    prior_mine = lax.dynamic_slice_in_dim(prior_state, own_start, own_count, 1)
    return prior_mine + increment


def solution(mesh):
    return jax.shard_map(
        shards,
        mesh=mesh,
        in_specs=(
            P(None, None, "tile"),
            P(("well", "tile"), None),
            P(("well", "tile"), None),
            P(("well", "tile")),
            P("tile", "well"),
            P("tile", "well"),
        ),
        out_specs=P(None, "well", "tile"),
        check_vma=False,
    )
```

```python
import jax
import jax.numpy as jnp
from jax import lax
from jax.sharding import PartitionSpec as P

BLOCK = 128


def chol_apply(system, right):
    factor = jnp.linalg.cholesky(system)
    middle = lax.linalg.triangular_solve(
        factor, right, left_side=True, lower=True, transpose_a=False
    )
    return lax.linalg.triangular_solve(factor, middle, left_side=True, lower=True, transpose_a=True)


def prepare(pred_rows, obs_rows, std_rows, norm_factor):
    data_anom = (pred_rows - jnp.mean(pred_rows, axis=1, keepdims=True)) * norm_factor
    innov = obs_rows - pred_rows
    row_weight = 1.0 / (4.0 * std_rows * std_rows)
    scaled = row_weight[:, None] * data_anom
    return (data_anom, innov, row_weight, scaled)


def bit_of(axis, k):
    return (lax.axis_index(axis) // k) % 2


def swap(x, axis, k):
    size = lax.axis_size(axis)
    return lax.ppermute(x, axis, [(i, i ^ k) for i in range(size)])


def axis_bits(axis):
    size = lax.axis_size(axis)
    out, k = [], 1
    while k < size:
        out.append((axis, k))
        k *= 2
    return out


def all_sum(x, steps):
    halved = []
    for axis, k in steps:
        rows = x.shape[0]
        if rows % 2 == 0:
            half = rows // 2
            hi = bit_of(axis, k) == 1
            keep = jnp.where(hi, x[half:], x[:half])
            send = jnp.where(hi, x[:half], x[half:])
            x = keep + swap(send, axis, k)
            halved.append((axis, k))
        else:
            x = x + swap(x, axis, k)
    for axis, k in reversed(halved):
        other = swap(x, axis, k)
        hi = bit_of(axis, k) == 1
        x = jnp.where(hi, jnp.concatenate([other, x], 0), jnp.concatenate([x, other], 0))
    return x


def well_reduce(full, split):
    for axis, k in reversed(axis_bits("well")):
        rows = split.shape[0]
        half = rows // 2
        hi = bit_of(axis, k) == 1
        keep = jnp.where(hi, split[half:], split[:half])
        send = jnp.where(hi, split[:half], split[half:])
        got = swap(jnp.concatenate([full, send], 0), axis, k)
        full = full + got[: full.shape[0]]
        split = keep + got[full.shape[0]:]
    return full, split


def shards(prior_state, pred_data, obs_pert, obs_std, loc_mask, taper_level):
    highest = lax.Precision.HIGHEST
    members = pred_data.shape[1]
    norm_factor = 1.0 / jnp.sqrt(jnp.float32(members - 1))
    data_anom, innov, row_weight, scaled = prepare(pred_data, obs_pert, obs_std, norm_factor)

    stacked = jnp.concatenate(
        [
            jnp.dot(data_anom.T, scaled, precision=highest),
            jnp.dot(scaled.T, innov, precision=highest),
        ],
        0,
    )
    order = axis_bits("tile")[:1] + axis_bits("well") + axis_bits("tile")[1:]
    stacked = all_sum(stacked, order)
    gram_matrix, cross_matrix = stacked[:members], stacked[members:]
    own_count = members // lax.axis_size("well")
    own_start = lax.axis_index("well") * own_count
    cross_mine = lax.dynamic_slice_in_dim(cross_matrix, own_start, own_count, 1)
    packed = jnp.concatenate([data_anom, innov, row_weight[:, None]], 1)
    group = lax.all_gather(packed, "tile", axis=0, tiled=True)
    group_anom, group_innov, group_weight = (
        group[:, :members],
        group[:, members : 2 * members],
        group[:, 2 * members],
    )
    taper_row = loc_mask[0].astype(jnp.float32) * taper_level[0].astype(jnp.float32) / 4.0
    row_taper = jnp.repeat(taper_row, BLOCK)
    tapered = (row_taper * group_weight)[:, None] * group_anom
    both = lax.dot_general(
        jnp.concatenate([group_anom, group_innov], 1),
        tapered,
        (((0,), (0,)), ((), ())),
        precision=highest,
    )
    taper_gram, taper_cross_t = both[:members], both[members:]
    taper_gram, cross_t_mine = well_reduce(taper_gram, taper_cross_t)
    gram_matrix, cross_mine, taper_gram, cross_t_mine = lax.optimization_barrier(
        (gram_matrix, cross_mine, taper_gram, cross_t_mine)
    )
    system = jnp.eye(members, dtype=jnp.float32) + gram_matrix
    solved_mine = chol_apply(system, cross_mine)

    space_t = cross_t_mine - lax.dot_general(
        solved_mine, taper_gram, (((0,), (1,)), ((), ())), precision=highest
    )
    state_anom = (prior_state - jnp.mean(prior_state, axis=1, keepdims=True)) * norm_factor
    increment = jnp.einsum("vnc,mn->vmc", state_anom, space_t, precision=highest)
    prior_mine = lax.dynamic_slice_in_dim(prior_state, own_start, own_count, 1)
    return prior_mine + increment


def solution(mesh):
    return jax.shard_map(
        shards,
        mesh=mesh,
        in_specs=(
            P(None, None, "tile"),
            P(("well", "tile"), None),
            P(("well", "tile"), None),
            P(("well", "tile")),
            P("tile", "well"),
            P("tile", "well"),
        ),
        out_specs=P(None, "well", "tile"),
        check_vma=False,
    )
```

```python
import jax
import jax.numpy as jnp
from jax import lax
from jax.sharding import PartitionSpec as P

BLOCK = 128


def prepare(pred_rows, obs_rows, std_rows, norm_factor):
    data_anom = (pred_rows - jnp.mean(pred_rows, axis=1, keepdims=True)) * norm_factor
    innov = obs_rows - pred_rows
    row_weight = 1.0 / (4.0 * std_rows * std_rows)
    scaled = row_weight[:, None] * data_anom
    return (data_anom, innov, row_weight, scaled)


def bit_of(axis, k):
    return (lax.axis_index(axis) // k) % 2


def swap(x, axis, k):
    size = lax.axis_size(axis)
    return lax.ppermute(x, axis, [(i, i ^ k) for i in range(size)])


def axis_bits(axis):
    size = lax.axis_size(axis)
    out, k = [], 1
    while k < size:
        out.append((axis, k))
        k *= 2
    return out


def all_sum(x, steps, tie):
    halved = []
    for axis, k in steps:
        rows = x.shape[0]
        if rows % 2 == 0:
            half = rows // 2
            hi = bit_of(axis, k) == 1
            keep = jnp.where(hi, x[half:], x[:half])
            send = jnp.where(hi, x[:half], x[half:])
            x = keep + swap(send, axis, k)
            halved.append((axis, k))
        else:
            x = x + swap(x, axis, k)
    x, tie = lax.optimization_barrier((x, tie))
    for axis, k in reversed(halved):
        other = swap(x, axis, k)
        hi = bit_of(axis, k) == 1
        x = jnp.where(hi, jnp.concatenate([other, x], 0), jnp.concatenate([x, other], 0))
    return x, tie


def well_step(full, split, axis, k):
    rows = split.shape[0]
    half = rows // 2
    hi = bit_of(axis, k) == 1
    keep = jnp.where(hi, split[half:], split[:half])
    send = jnp.where(hi, split[:half], split[half:])
    got = swap(jnp.concatenate([full, send], 0), axis, k)
    return full + got[: full.shape[0]], keep + got[full.shape[0]:]


def shards(prior_state, pred_data, obs_pert, obs_std, loc_mask, taper_level):
    highest = lax.Precision.HIGHEST
    members = pred_data.shape[1]
    norm_factor = 1.0 / jnp.sqrt(jnp.float32(members - 1))
    data_anom, innov, row_weight, scaled = prepare(pred_data, obs_pert, obs_std, norm_factor)

    stacked = jnp.concatenate(
        [
            jnp.dot(data_anom.T, scaled, precision=highest),
            jnp.dot(scaled.T, innov, precision=highest),
        ],
        0,
    )
    packed = jnp.concatenate([data_anom, innov, row_weight[:, None]], 1)
    order = axis_bits("tile")[:1] + axis_bits("well") + axis_bits("tile")[1:]
    stacked, packed = all_sum(stacked, order, packed)
    gram_matrix, cross_matrix = stacked[:members], stacked[members:]
    own_count = members // lax.axis_size("well")
    own_start = lax.axis_index("well") * own_count
    cross_mine = lax.dynamic_slice_in_dim(cross_matrix, own_start, own_count, 1)
    system = jnp.eye(members, dtype=jnp.float32) + gram_matrix
    factor = jnp.linalg.cholesky(system)

    group = lax.all_gather(packed, "tile", axis=0, tiled=True)
    factor, group = lax.optimization_barrier((factor, group))
    group_anom, group_innov, group_weight = (
        group[:, :members],
        group[:, members : 2 * members],
        group[:, 2 * members],
    )
    taper_row = loc_mask[0].astype(jnp.float32) * taper_level[0].astype(jnp.float32) / 4.0
    row_taper = jnp.repeat(taper_row, BLOCK)
    tapered = (row_taper * group_weight)[:, None] * group_anom
    both = lax.dot_general(
        jnp.concatenate([group_anom, group_innov], 1),
        tapered,
        (((0,), (0,)), ((), ())),
        precision=highest,
    )
    taper_gram, taper_cross_t = both[:members], both[members:]
    steps = list(reversed(axis_bits("well")))
    factor, taper_gram, taper_cross_t = lax.optimization_barrier((factor, taper_gram, taper_cross_t))
    taper_gram, cross_t_mine = well_step(taper_gram, taper_cross_t, *steps[0])
    middle = lax.linalg.triangular_solve(
        factor, cross_mine, left_side=True, lower=True, transpose_a=False
    )
    middle, taper_gram, cross_t_mine = lax.optimization_barrier((middle, taper_gram, cross_t_mine))
    for axis, k in steps[1:]:
        taper_gram, cross_t_mine = well_step(taper_gram, cross_t_mine, axis, k)
    solved_mine = lax.linalg.triangular_solve(
        factor, middle, left_side=True, lower=True, transpose_a=True
    )

    space_t = cross_t_mine - lax.dot_general(
        solved_mine, taper_gram, (((0,), (1,)), ((), ())), precision=highest
    )
    state_anom = (prior_state - jnp.mean(prior_state, axis=1, keepdims=True)) * norm_factor
    increment = jnp.einsum("vnc,mn->vmc", state_anom, space_t, precision=highest)
    prior_mine = lax.dynamic_slice_in_dim(prior_state, own_start, own_count, 1)
    return prior_mine + increment


def solution(mesh):
    return jax.shard_map(
        shards,
        mesh=mesh,
        in_specs=(
            P(None, None, "tile"),
            P(("well", "tile"), None),
            P(("well", "tile"), None),
            P(("well", "tile")),
            P("tile", "well"),
            P("tile", "well"),
        ),
        out_specs=P(None, "well", "tile"),
        check_vma=False,
    )
```

```python
import jax
import jax.numpy as jnp
from jax import lax
from jax.sharding import PartitionSpec as P

BLOCK = 128


def prepare(pred_rows, obs_rows, std_rows, norm_factor):
    data_anom = (pred_rows - jnp.mean(pred_rows, axis=1, keepdims=True)) * norm_factor
    innov = obs_rows - pred_rows
    row_weight = 1.0 / (4.0 * std_rows * std_rows)
    scaled = row_weight[:, None] * data_anom
    return (data_anom, innov, row_weight, scaled)


def bit_of(axis, k):
    return (lax.axis_index(axis) // k) % 2


def swap(x, axis, k):
    size = lax.axis_size(axis)
    return lax.ppermute(x, axis, [(i, i ^ k) for i in range(size)])


def axis_bits(axis):
    size = lax.axis_size(axis)
    out, k = [], 1
    while k < size:
        out.append((axis, k))
        k *= 2
    return out


def all_sum(x, steps, tie):
    halved = []
    for axis, k in steps:
        rows = x.shape[0]
        if rows % 2 == 0:
            half = rows // 2
            hi = bit_of(axis, k) == 1
            keep = jnp.where(hi, x[half:], x[:half])
            send = jnp.where(hi, x[:half], x[half:])
            x = keep + swap(send, axis, k)
            halved.append((axis, k))
        else:
            x = x + swap(x, axis, k)
    x, tie = lax.optimization_barrier((x, tie))
    for axis, k in reversed(halved):
        other = swap(x, axis, k)
        hi = bit_of(axis, k) == 1
        x = jnp.where(hi, jnp.concatenate([other, x], 0), jnp.concatenate([x, other], 0))
    return x, tie


def well_step(full, split, axis, k):
    rows = split.shape[0]
    half = rows // 2
    hi = bit_of(axis, k) == 1
    keep = jnp.where(hi, split[half:], split[:half])
    send = jnp.where(hi, split[:half], split[half:])
    got = swap(jnp.concatenate([full, send], 0), axis, k)
    return full + got[: full.shape[0]], keep + got[full.shape[0]:]


def line_gather(packed, taper_row):
    size = lax.axis_size("tile")
    me = lax.axis_index("tile")
    chips = size // 2
    z = me // 2
    rows = packed.shape[0]
    partner_row = swap(taper_row, "tile", 1)
    left, right = [packed], [packed]
    for _ in range(1, chips):
        left.append(lax.ppermute(left[-1], "tile", [(i, i + 2) for i in range(size - 2)]))
        right.append(lax.ppermute(right[-1], "tile", [(i, i - 2) for i in range(2, size)]))
    pieces, sources = [packed], [me]
    for k in range(1, chips):
        ahead = z + k <= chips - 1
        pieces.append(jnp.where(ahead, right[k], left[chips - k]))
        sources.append(jnp.where(ahead, me + 2 * k, me - 2 * (chips - k)))
    row_tapers = []
    for row in (taper_row, partner_row):
        per_piece = [
            jnp.broadcast_to(lax.dynamic_index_in_dim(row, (src * rows) // BLOCK, 0, False), (rows,))
            for src in sources
        ]
        row_tapers.append(jnp.concatenate(per_piece, 0))
    return pieces, row_tapers


def tapered_sums(pieces, row_tapers, members, precision):
    group = jnp.concatenate(pieces, 0)
    anom, innov, weight = group[:, :members], group[:, members : 2 * members], group[:, 2 * members]
    cols = [(row_taper * weight)[:, None] * anom for row_taper in row_tapers]
    return lax.dot_general(
        jnp.concatenate([anom, innov], 1),
        jnp.concatenate(cols, 1),
        (((0,), (0,)), ((), ())),
        precision=precision,
    )


def shards(prior_state, pred_data, obs_pert, obs_std, loc_mask, taper_level):
    highest = lax.Precision.HIGHEST
    members = pred_data.shape[1]
    norm_factor = 1.0 / jnp.sqrt(jnp.float32(members - 1))
    data_anom, innov, row_weight, scaled = prepare(pred_data, obs_pert, obs_std, norm_factor)

    stacked = jnp.concatenate(
        [
            jnp.dot(data_anom.T, scaled, precision=highest),
            jnp.dot(scaled.T, innov, precision=highest),
        ],
        0,
    )
    packed = jnp.concatenate([data_anom, innov, row_weight[:, None]], 1)
    order = axis_bits("tile")[:1] + axis_bits("well") + axis_bits("tile")[1:]
    stacked, packed = all_sum(stacked, order, packed)
    gram_matrix, cross_matrix = stacked[:members], stacked[members:]
    own_count = members // lax.axis_size("well")
    own_start = lax.axis_index("well") * own_count
    cross_mine = lax.dynamic_slice_in_dim(cross_matrix, own_start, own_count, 1)
    system = jnp.eye(members, dtype=jnp.float32) + gram_matrix
    factor = jnp.linalg.cholesky(system)

    taper_row = loc_mask[0].astype(jnp.float32) * taper_level[0].astype(jnp.float32) / 4.0
    if lax.axis_size("tile") == 8:
        pieces, weights = line_gather(packed, taper_row)
        factor, pieces = lax.optimization_barrier((factor, pieces))
        both = tapered_sums(pieces, weights, members, highest)
        mine, theirs = both[:, :members], both[:, members:]
        both = mine + swap(theirs, "tile", 1)
    else:
        group = lax.all_gather(packed, "tile", axis=0, tiled=True)
        factor, group = lax.optimization_barrier((factor, group))
        row_taper = jnp.repeat(taper_row, BLOCK)
        both = tapered_sums([group], [row_taper], members, highest)
    taper_gram, taper_cross_t = both[:members], both[members:]
    factor, taper_gram, taper_cross_t = lax.optimization_barrier((factor, taper_gram, taper_cross_t))

    steps = list(reversed(axis_bits("well")))
    taper_gram, cross_t_mine = well_step(taper_gram, taper_cross_t, *steps[0])
    middle = lax.linalg.triangular_solve(
        factor, cross_mine, left_side=True, lower=True, transpose_a=False
    )
    middle, taper_gram, cross_t_mine = lax.optimization_barrier((middle, taper_gram, cross_t_mine))
    for axis, k in steps[1:]:
        taper_gram, cross_t_mine = well_step(taper_gram, cross_t_mine, axis, k)
    solved_mine = lax.linalg.triangular_solve(
        factor, middle, left_side=True, lower=True, transpose_a=True
    )

    space_t = cross_t_mine - lax.dot_general(
        solved_mine, taper_gram, (((0,), (1,)), ((), ())), precision=highest
    )
    state_anom = (prior_state - jnp.mean(prior_state, axis=1, keepdims=True)) * norm_factor
    increment = jnp.einsum("vnc,mn->vmc", state_anom, space_t, precision=highest)
    prior_mine = lax.dynamic_slice_in_dim(prior_state, own_start, own_count, 1)
    return prior_mine + increment


def solution(mesh):
    return jax.shard_map(
        shards,
        mesh=mesh,
        in_specs=(
            P(None, None, "tile"),
            P(("well", "tile"), None),
            P(("well", "tile"), None),
            P(("well", "tile")),
            P("tile", "well"),
            P("tile", "well"),
        ),
        out_specs=P(None, "well", "tile"),
        check_vma=False,
    )
```

```python
import jax
import jax.numpy as jnp
from jax import lax
from jax.sharding import PartitionSpec as P

BLOCK = 128


def lower_inverse(factor, precision):
    eye = jnp.eye(factor.shape[0], dtype=factor.dtype)
    return lax.linalg.triangular_solve(factor, eye, left_side=True, lower=True, transpose_a=False)


def block_cholesky(system, split, precision):
    system = (system + system.T) * 0.5
    a11, a21, a22 = system[:split, :split], system[split:, :split], system[split:, split:]
    l11 = lax.linalg.cholesky(a11, symmetrize_input=False)
    inv11 = lower_inverse(l11, precision)
    l21 = jnp.dot(a21, inv11.T, precision=precision)
    l22 = lax.linalg.cholesky(a22 - jnp.dot(l21, l21.T, precision=precision), symmetrize_input=False)
    inv22 = lower_inverse(l22, precision)
    return inv11, l21, inv22


def forward(parts, right, precision):
    inv11, l21, inv22 = parts
    split = inv11.shape[0]
    y1 = jnp.dot(inv11, right[:split], precision=precision)
    y2 = jnp.dot(inv22, right[split:] - jnp.dot(l21, y1, precision=precision), precision=precision)
    return y1, y2


def backward(parts, y1, y2, precision):
    inv11, l21, inv22 = parts
    x2 = jnp.dot(inv22.T, y2, precision=precision)
    x1 = jnp.dot(inv11.T, y1 - jnp.dot(l21.T, x2, precision=precision), precision=precision)
    return jnp.concatenate([x1, x2], 0)


def prepare(pred_rows, obs_rows, std_rows, norm_factor):
    data_anom = (pred_rows - jnp.mean(pred_rows, axis=1, keepdims=True)) * norm_factor
    innov = obs_rows - pred_rows
    row_weight = 1.0 / (4.0 * std_rows * std_rows)
    scaled = row_weight[:, None] * data_anom
    return (data_anom, innov, row_weight, scaled)


def bit_of(axis, k):
    return (lax.axis_index(axis) // k) % 2


def swap(x, axis, k):
    size = lax.axis_size(axis)
    return lax.ppermute(x, axis, [(i, i ^ k) for i in range(size)])


def axis_bits(axis):
    size = lax.axis_size(axis)
    out, k = [], 1
    while k < size:
        out.append((axis, k))
        k *= 2
    return out


def all_sum(x, steps, tie):
    halved = []
    for axis, k in steps:
        rows = x.shape[0]
        if rows % 2 == 0:
            half = rows // 2
            hi = bit_of(axis, k) == 1
            keep = jnp.where(hi, x[half:], x[:half])
            send = jnp.where(hi, x[:half], x[half:])
            x = keep + swap(send, axis, k)
            halved.append((axis, k))
        else:
            x = x + swap(x, axis, k)
    x, tie = lax.optimization_barrier((x, tie))
    for axis, k in reversed(halved):
        other = swap(x, axis, k)
        hi = bit_of(axis, k) == 1
        x = jnp.where(hi, jnp.concatenate([other, x], 0), jnp.concatenate([x, other], 0))
    return x, tie


def well_step(full, split, axis, k):
    rows = split.shape[0]
    half = rows // 2
    hi = bit_of(axis, k) == 1
    keep = jnp.where(hi, split[half:], split[:half])
    send = jnp.where(hi, split[:half], split[half:])
    got = swap(jnp.concatenate([full, send], 0), axis, k)
    return full + got[: full.shape[0]], keep + got[full.shape[0]:]


def shards(prior_state, pred_data, obs_pert, obs_std, loc_mask, taper_level):
    highest = lax.Precision.HIGHEST
    members = pred_data.shape[1]
    norm_factor = 1.0 / jnp.sqrt(jnp.float32(members - 1))
    data_anom, innov, row_weight, scaled = prepare(pred_data, obs_pert, obs_std, norm_factor)

    stacked = jnp.concatenate(
        [
            jnp.dot(data_anom.T, scaled, precision=highest),
            jnp.dot(scaled.T, innov, precision=highest),
        ],
        0,
    )
    packed = jnp.concatenate([data_anom, innov, row_weight[:, None]], 1)
    order = axis_bits("tile")[:1] + axis_bits("well") + axis_bits("tile")[1:]
    stacked, packed = all_sum(stacked, order, packed)
    gram_matrix, cross_matrix = stacked[:members], stacked[members:]
    own_count = members // lax.axis_size("well")
    own_start = lax.axis_index("well") * own_count
    cross_mine = lax.dynamic_slice_in_dim(cross_matrix, own_start, own_count, 1)
    system = jnp.eye(members, dtype=jnp.float32) + gram_matrix
    factor = block_cholesky(system, min(BLOCK, members - 8), highest)

    group = lax.all_gather(packed, "tile", axis=0, tiled=True)
    factor, group = lax.optimization_barrier((factor, group))
    group_anom, group_innov, group_weight = (
        group[:, :members],
        group[:, members : 2 * members],
        group[:, 2 * members],
    )
    taper_row = loc_mask[0].astype(jnp.float32) * taper_level[0].astype(jnp.float32) / 4.0
    row_taper = jnp.repeat(taper_row, BLOCK)
    tapered = (row_taper * group_weight)[:, None] * group_anom
    both = lax.dot_general(
        jnp.concatenate([group_anom, group_innov], 1),
        tapered,
        (((0,), (0,)), ((), ())),
        precision=highest,
    )
    taper_gram, taper_cross_t = both[:members], both[members:]
    steps = list(reversed(axis_bits("well")))
    factor, taper_gram, taper_cross_t = lax.optimization_barrier((factor, taper_gram, taper_cross_t))
    taper_gram, cross_t_mine = well_step(taper_gram, taper_cross_t, *steps[0])
    middle = forward(factor, cross_mine, highest)
    middle, taper_gram, cross_t_mine = lax.optimization_barrier((middle, taper_gram, cross_t_mine))
    for axis, k in steps[1:]:
        taper_gram, cross_t_mine = well_step(taper_gram, cross_t_mine, axis, k)
    solved_mine = backward(factor, *middle, highest)

    space_t = cross_t_mine - lax.dot_general(
        solved_mine, taper_gram, (((0,), (1,)), ((), ())), precision=highest
    )
    state_anom = (prior_state - jnp.mean(prior_state, axis=1, keepdims=True)) * norm_factor
    increment = jnp.einsum("vnc,mn->vmc", state_anom, space_t, precision=highest)
    prior_mine = lax.dynamic_slice_in_dim(prior_state, own_start, own_count, 1)
    return prior_mine + increment


def solution(mesh):
    return jax.shard_map(
        shards,
        mesh=mesh,
        in_specs=(
            P(None, None, "tile"),
            P(("well", "tile"), None),
            P(("well", "tile"), None),
            P(("well", "tile")),
            P("tile", "well"),
            P("tile", "well"),
        ),
        out_specs=P(None, "well", "tile"),
        check_vma=False,
    )
```

```python
import jax
import jax.numpy as jnp
from jax import lax
from jax.sharding import PartitionSpec as P

BLOCK = 128


def lower_inverse(factor, precision):
    eye = jnp.eye(factor.shape[0], dtype=factor.dtype)
    return lax.linalg.triangular_solve(factor, eye, left_side=True, lower=True, transpose_a=False)


def block_cholesky(system, split, precision):
    system = (system + system.T) * 0.5
    a11, a21, a22 = system[:split, :split], system[split:, :split], system[split:, split:]
    l11 = lax.linalg.cholesky(a11, symmetrize_input=False)
    inv11 = lower_inverse(l11, precision)
    l21 = jnp.dot(a21, inv11.T, precision=precision)
    l22 = lax.linalg.cholesky(a22 - jnp.dot(l21, l21.T, precision=precision), symmetrize_input=False)
    inv22 = lower_inverse(l22, precision)
    return inv11, l21, inv22


def forward(parts, right, precision):
    inv11, l21, inv22 = parts
    split = inv11.shape[0]
    y1 = jnp.dot(inv11, right[:split], precision=precision)
    y2 = jnp.dot(inv22, right[split:] - jnp.dot(l21, y1, precision=precision), precision=precision)
    return y1, y2


def backward(parts, y1, y2, precision):
    inv11, l21, inv22 = parts
    x2 = jnp.dot(inv22.T, y2, precision=precision)
    x1 = jnp.dot(inv11.T, y1 - jnp.dot(l21.T, x2, precision=precision), precision=precision)
    return jnp.concatenate([x1, x2], 0)


def prepare(pred_rows, obs_rows, std_rows, norm_factor):
    data_anom = (pred_rows - jnp.mean(pred_rows, axis=1, keepdims=True)) * norm_factor
    innov = obs_rows - pred_rows
    row_weight = 1.0 / (4.0 * std_rows * std_rows)
    scaled = row_weight[:, None] * data_anom
    return (data_anom, innov, row_weight, scaled)


def bit_of(axis, k):
    return (lax.axis_index(axis) // k) % 2


def swap(x, axis, k):
    size = lax.axis_size(axis)
    return lax.ppermute(x, axis, [(i, i ^ k) for i in range(size)])


def axis_bits(axis):
    size = lax.axis_size(axis)
    out, k = [], 1
    while k < size:
        out.append((axis, k))
        k *= 2
    return out


def all_sum(x, steps, tie):
    halved = []
    for axis, k in steps:
        rows = x.shape[0]
        if rows % 2 == 0:
            half = rows // 2
            hi = bit_of(axis, k) == 1
            keep = jnp.where(hi, x[half:], x[:half])
            send = jnp.where(hi, x[:half], x[half:])
            x = keep + swap(send, axis, k)
            halved.append((axis, k))
        else:
            x = x + swap(x, axis, k)
    x, tie = lax.optimization_barrier((x, tie))
    for axis, k in reversed(halved):
        other = swap(x, axis, k)
        hi = bit_of(axis, k) == 1
        x = jnp.where(hi, jnp.concatenate([other, x], 0), jnp.concatenate([x, other], 0))
    return x, tie


def shards(prior_state, pred_data, obs_pert, obs_std, loc_mask, taper_level):
    highest = lax.Precision.HIGHEST
    members = pred_data.shape[1]
    norm_factor = 1.0 / jnp.sqrt(jnp.float32(members - 1))
    data_anom, innov, row_weight, scaled = prepare(pred_data, obs_pert, obs_std, norm_factor)

    stacked = jnp.concatenate(
        [
            jnp.dot(data_anom.T, scaled, precision=highest),
            jnp.dot(scaled.T, innov, precision=highest),
        ],
        0,
    )
    packed = jnp.concatenate([data_anom, innov, row_weight[:, None]], 1)
    order = axis_bits("tile")[:1] + axis_bits("well") + axis_bits("tile")[1:]
    stacked, packed = all_sum(stacked, order, packed)
    gram_matrix, cross_matrix = stacked[:members], stacked[members:]
    own_count = members // lax.axis_size("well")
    own_start = lax.axis_index("well") * own_count
    system = jnp.eye(members, dtype=jnp.float32) + gram_matrix
    factor = block_cholesky(system, min(BLOCK, members - 8), highest)

    group = lax.all_gather(packed, "tile", axis=0, tiled=True)
    factor, group = lax.optimization_barrier((factor, group))
    group_anom, group_innov, group_weight = (
        group[:, :members],
        group[:, members : 2 * members],
        group[:, 2 * members],
    )
    taper_row = loc_mask[0].astype(jnp.float32) * taper_level[0].astype(jnp.float32) / 4.0
    row_taper = jnp.repeat(taper_row, BLOCK)
    tapered = (row_taper * group_weight)[:, None] * group_anom
    both = lax.dot_general(
        jnp.concatenate([group_anom, group_innov], 1),
        tapered,
        (((0,), (0,)), ((), ())),
        precision=highest,
    )
    taper_gram, taper_cross_t = both[:members], both[members:]

    solved = backward(factor, *forward(factor, cross_matrix, highest), highest)
    space_t = taper_cross_t - lax.dot_general(
        solved, taper_gram, (((0,), (1,)), ((), ())), precision=highest
    )
    for axis, k in reversed(axis_bits("well")):
        half = space_t.shape[0] // 2
        hi = bit_of(axis, k) == 1
        keep = jnp.where(hi, space_t[half:], space_t[:half])
        send = jnp.where(hi, space_t[:half], space_t[half:])
        space_t = keep + swap(send, axis, k)
    state_anom = (prior_state - jnp.mean(prior_state, axis=1, keepdims=True)) * norm_factor
    increment = jnp.einsum("vnc,mn->vmc", state_anom, space_t, precision=highest)
    prior_mine = lax.dynamic_slice_in_dim(prior_state, own_start, own_count, 1)
    return prior_mine + increment


def solution(mesh):
    return jax.shard_map(
        shards,
        mesh=mesh,
        in_specs=(
            P(None, None, "tile"),
            P(("well", "tile"), None),
            P(("well", "tile"), None),
            P(("well", "tile")),
            P("tile", "well"),
            P("tile", "well"),
        ),
        out_specs=P(None, "well", "tile"),
        check_vma=False,
    )
```

```python
import jax
import jax.numpy as jnp
from jax import lax
from jax.sharding import PartitionSpec as P

BLOCK = 128


def lower_inverse(factor, precision):
    eye = jnp.eye(factor.shape[0], dtype=factor.dtype)
    return lax.linalg.triangular_solve(factor, eye, left_side=True, lower=True, transpose_a=False)


def block_cholesky(system, split, precision):
    system = (system + system.T) * 0.5
    a11, a21, a22 = system[:split, :split], system[split:, :split], system[split:, split:]
    l11 = lax.linalg.cholesky(a11, symmetrize_input=False)
    inv11 = lower_inverse(l11, precision)
    l21 = jnp.dot(a21, inv11.T, precision=precision)
    l22 = lax.linalg.cholesky(a22 - jnp.dot(l21, l21.T, precision=precision), symmetrize_input=False)
    inv22 = lower_inverse(l22, precision)
    return inv11, l21, inv22


def forward(parts, right, precision):
    inv11, l21, inv22 = parts
    split = inv11.shape[0]
    y1 = jnp.dot(inv11, right[:split], precision=precision)
    y2 = jnp.dot(inv22, right[split:] - jnp.dot(l21, y1, precision=precision), precision=precision)
    return y1, y2


def backward(parts, y1, y2, precision):
    inv11, l21, inv22 = parts
    x2 = jnp.dot(inv22.T, y2, precision=precision)
    x1 = jnp.dot(inv11.T, y1 - jnp.dot(l21.T, x2, precision=precision), precision=precision)
    return jnp.concatenate([x1, x2], 0)


def prepare(pred_rows, obs_rows, std_rows, norm_factor):
    data_anom = (pred_rows - jnp.mean(pred_rows, axis=1, keepdims=True)) * norm_factor
    innov = obs_rows - pred_rows
    row_weight = 1.0 / (4.0 * std_rows * std_rows)
    scaled = row_weight[:, None] * data_anom
    return (data_anom, innov, row_weight, scaled)


def bit_of(axis, k):
    return (lax.axis_index(axis) // k) % 2


def swap(x, axis, k):
    size = lax.axis_size(axis)
    return lax.ppermute(x, axis, [(i, i ^ k) for i in range(size)])


def axis_bits(axis):
    size = lax.axis_size(axis)
    out, k = [], 1
    while k < size:
        out.append((axis, k))
        k *= 2
    return out


def all_sum(x, steps, tie):
    halved = []
    for axis, k in steps:
        rows = x.shape[0]
        if rows % 2 == 0:
            half = rows // 2
            hi = bit_of(axis, k) == 1
            keep = jnp.where(hi, x[half:], x[:half])
            send = jnp.where(hi, x[:half], x[half:])
            x = keep + swap(send, axis, k)
            halved.append((axis, k))
        else:
            x = x + swap(x, axis, k)
    x, tie = lax.optimization_barrier((x, tie))
    for axis, k in reversed(halved):
        other = swap(x, axis, k)
        hi = bit_of(axis, k) == 1
        x = jnp.where(hi, jnp.concatenate([other, x], 0), jnp.concatenate([x, other], 0))
    return x, tie


def shards(prior_state, pred_data, obs_pert, obs_std, loc_mask, taper_level):
    highest = lax.Precision.HIGHEST
    members = pred_data.shape[1]
    norm_factor = 1.0 / jnp.sqrt(jnp.float32(members - 1))
    data_anom, innov, row_weight, scaled = prepare(pred_data, obs_pert, obs_std, norm_factor)

    stacked = jnp.concatenate(
        [
            jnp.dot(data_anom.T, scaled, precision=highest),
            jnp.dot(scaled.T, innov, precision=highest),
        ],
        0,
    )
    packed = jnp.concatenate([data_anom, innov, row_weight[:, None]], 1)
    order = axis_bits("tile")[:1] + axis_bits("well") + axis_bits("tile")[1:]
    stacked, packed = all_sum(stacked, order, packed)
    gram_matrix, cross_matrix = stacked[:members], stacked[members:]
    own_count = members // lax.axis_size("well")
    own_start = lax.axis_index("well") * own_count
    system = jnp.eye(members, dtype=jnp.float32) + gram_matrix
    factor = block_cholesky(system, min(BLOCK, members - 8), highest)

    copies = jnp.broadcast_to(packed[None], (lax.axis_size("tile"),) + packed.shape)
    group = lax.all_to_all(copies, "tile", 0, 0, tiled=False).reshape((-1, packed.shape[1]))
    factor, group = lax.optimization_barrier((factor, group))
    group_anom, group_innov, group_weight = (
        group[:, :members],
        group[:, members : 2 * members],
        group[:, 2 * members],
    )
    taper_row = loc_mask[0].astype(jnp.float32) * taper_level[0].astype(jnp.float32) / 4.0
    row_taper = jnp.repeat(taper_row, BLOCK)
    tapered = (row_taper * group_weight)[:, None] * group_anom
    both = lax.dot_general(
        jnp.concatenate([group_anom, group_innov], 1),
        tapered,
        (((0,), (0,)), ((), ())),
        precision=highest,
    )
    taper_gram, taper_cross_t = both[:members], both[members:]

    solved = backward(factor, *forward(factor, cross_matrix, highest), highest)
    space_t = taper_cross_t - lax.dot_general(
        solved, taper_gram, (((0,), (1,)), ((), ())), precision=highest
    )
    for axis, k in reversed(axis_bits("well")):
        half = space_t.shape[0] // 2
        hi = bit_of(axis, k) == 1
        keep = jnp.where(hi, space_t[half:], space_t[:half])
        send = jnp.where(hi, space_t[:half], space_t[half:])
        space_t = keep + swap(send, axis, k)
    state_anom = (prior_state - jnp.mean(prior_state, axis=1, keepdims=True)) * norm_factor
    increment = jnp.einsum("vnc,mn->vmc", state_anom, space_t, precision=highest)
    prior_mine = lax.dynamic_slice_in_dim(prior_state, own_start, own_count, 1)
    return prior_mine + increment


def solution(mesh):
    return jax.shard_map(
        shards,
        mesh=mesh,
        in_specs=(
            P(None, None, "tile"),
            P(("well", "tile"), None),
            P(("well", "tile"), None),
            P(("well", "tile")),
            P("tile", "well"),
            P("tile", "well"),
        ),
        out_specs=P(None, "well", "tile"),
        check_vma=False,
    )
```

```python
import jax
import jax.numpy as jnp
from jax import lax
from jax.sharding import PartitionSpec as P

BLOCK = 128


def lower_inverse(factor, precision):
    eye = jnp.eye(factor.shape[0], dtype=factor.dtype)
    return lax.linalg.triangular_solve(factor, eye, left_side=True, lower=True, transpose_a=False)


def block_cholesky(system, split, precision):
    system = (system + system.T) * 0.5
    a11, a21, a22 = system[:split, :split], system[split:, :split], system[split:, split:]
    l11 = lax.linalg.cholesky(a11, symmetrize_input=False)
    inv11 = lower_inverse(l11, precision)
    l21 = jnp.dot(a21, inv11.T, precision=precision)
    l22 = lax.linalg.cholesky(a22 - jnp.dot(l21, l21.T, precision=precision), symmetrize_input=False)
    inv22 = lower_inverse(l22, precision)
    return inv11, l21, inv22


def forward(parts, right, precision):
    inv11, l21, inv22 = parts
    split = inv11.shape[0]
    y1 = jnp.dot(inv11, right[:split], precision=precision)
    y2 = jnp.dot(inv22, right[split:] - jnp.dot(l21, y1, precision=precision), precision=precision)
    return y1, y2


def backward(parts, y1, y2, precision):
    inv11, l21, inv22 = parts
    x2 = jnp.dot(inv22.T, y2, precision=precision)
    x1 = jnp.dot(inv11.T, y1 - jnp.dot(l21.T, x2, precision=precision), precision=precision)
    return jnp.concatenate([x1, x2], 0)


def prepare(pred_rows, obs_rows, std_rows, norm_factor):
    data_anom = (pred_rows - jnp.mean(pred_rows, axis=1, keepdims=True)) * norm_factor
    innov = obs_rows - pred_rows
    row_weight = 1.0 / (4.0 * std_rows * std_rows)
    scaled = row_weight[:, None] * data_anom
    return (data_anom, innov, row_weight, scaled)


def bit_of(axis, k):
    return (lax.axis_index(axis) // k) % 2


def swap(x, axis, k):
    size = lax.axis_size(axis)
    return lax.ppermute(x, axis, [(i, i ^ k) for i in range(size)])


def axis_bits(axis):
    size = lax.axis_size(axis)
    out, k = [], 1
    while k < size:
        out.append((axis, k))
        k *= 2
    return out


def all_sum(x, steps, halvings, tie):
    for axis, k in steps[:halvings]:
        half = x.shape[0] // 2
        hi = bit_of(axis, k) == 1
        keep = jnp.where(hi, x[half:], x[:half])
        send = jnp.where(hi, x[:half], x[half:])
        x = keep + swap(send, axis, k)
    for axis, k in steps[halvings:]:
        x = x + swap(x, axis, k)
    x, tie = lax.optimization_barrier((x, tie))
    for axis, k in reversed(steps[:halvings]):
        other = swap(x, axis, k)
        hi = bit_of(axis, k) == 1
        x = jnp.where(hi, jnp.concatenate([other, x], 0), jnp.concatenate([x, other], 0))
    return x, tie


def shards(prior_state, pred_data, obs_pert, obs_std, loc_mask, taper_level):
    highest = lax.Precision.HIGHEST
    members = pred_data.shape[1]
    norm_factor = 1.0 / jnp.sqrt(jnp.float32(members - 1))
    data_anom, innov, row_weight, scaled = prepare(pred_data, obs_pert, obs_std, norm_factor)

    stacked = jnp.concatenate(
        [
            jnp.dot(data_anom.T, scaled, precision=highest),
            jnp.dot(scaled.T, innov, precision=highest),
        ],
        0,
    )
    packed = jnp.concatenate([data_anom, innov, row_weight[:, None]], 1)
    order = axis_bits("tile")[:1] + axis_bits("well") + axis_bits("tile")[1:]
    stacked, packed = all_sum(stacked, order, 2, packed)
    gram_matrix, cross_matrix = stacked[:members], stacked[members:]
    own_count = members // lax.axis_size("well")
    own_start = lax.axis_index("well") * own_count
    system = jnp.eye(members, dtype=jnp.float32) + gram_matrix
    factor = block_cholesky(system, min(BLOCK, members - 8), highest)

    copies = jnp.broadcast_to(packed[None], (lax.axis_size("tile"),) + packed.shape)
    group = lax.all_to_all(copies, "tile", 0, 0, tiled=False).reshape((-1, packed.shape[1]))
    factor, group = lax.optimization_barrier((factor, group))
    group_anom, group_innov, group_weight = (
        group[:, :members],
        group[:, members : 2 * members],
        group[:, 2 * members],
    )
    taper_row = loc_mask[0].astype(jnp.float32) * taper_level[0].astype(jnp.float32) / 4.0
    row_taper = jnp.repeat(taper_row, BLOCK)
    tapered = (row_taper * group_weight)[:, None] * group_anom
    both = lax.dot_general(
        jnp.concatenate([group_anom, group_innov], 1),
        tapered,
        (((0,), (0,)), ((), ())),
        precision=highest,
    )
    taper_gram, taper_cross_t = both[:members], both[members:]

    solved = backward(factor, *forward(factor, cross_matrix, highest), highest)
    space_t = taper_cross_t - lax.dot_general(
        solved, taper_gram, (((0,), (1,)), ((), ())), precision=highest
    )
    for axis, k in reversed(axis_bits("well")):
        half = space_t.shape[0] // 2
        hi = bit_of(axis, k) == 1
        keep = jnp.where(hi, space_t[half:], space_t[:half])
        send = jnp.where(hi, space_t[:half], space_t[half:])
        space_t = keep + swap(send, axis, k)
    state_anom = (prior_state - jnp.mean(prior_state, axis=1, keepdims=True)) * norm_factor
    increment = jnp.einsum("vnc,mn->vmc", state_anom, space_t, precision=highest)
    prior_mine = lax.dynamic_slice_in_dim(prior_state, own_start, own_count, 1)
    return prior_mine + increment


def solution(mesh):
    return jax.shard_map(
        shards,
        mesh=mesh,
        in_specs=(
            P(None, None, "tile"),
            P(("well", "tile"), None),
            P(("well", "tile"), None),
            P(("well", "tile")),
            P("tile", "well"),
            P("tile", "well"),
        ),
        out_specs=P(None, "well", "tile"),
        check_vma=False,
    )
```

```python
import jax
import jax.numpy as jnp
from jax import lax
from jax.sharding import PartitionSpec as P

BLOCK = 128


def lower_inverse(factor, precision):
    eye = jnp.eye(factor.shape[0], dtype=factor.dtype)
    return lax.linalg.triangular_solve(factor, eye, left_side=True, lower=True, transpose_a=False)


def block_cholesky(system, split, precision):
    system = (system + system.T) * 0.5
    a11, a21, a22 = system[:split, :split], system[split:, :split], system[split:, split:]
    l11 = lax.linalg.cholesky(a11, symmetrize_input=False)
    inv11 = lower_inverse(l11, precision)
    l21 = jnp.dot(a21, inv11.T, precision=precision)
    l22 = lax.linalg.cholesky(a22 - jnp.dot(l21, l21.T, precision=precision), symmetrize_input=False)
    return inv11, l21, l22


def forward(parts, right, precision):
    inv11, l21, inv22 = parts
    split = inv11.shape[0]
    y1 = jnp.dot(inv11, right[:split], precision=precision)
    y2 = jnp.dot(inv22, right[split:] - jnp.dot(l21, y1, precision=precision), precision=precision)
    return y1, y2


def backward(parts, y1, y2, precision):
    inv11, l21, inv22 = parts
    x2 = jnp.dot(inv22.T, y2, precision=precision)
    x1 = jnp.dot(inv11.T, y1 - jnp.dot(l21.T, x2, precision=precision), precision=precision)
    return jnp.concatenate([x1, x2], 0)


def prepare(pred_rows, obs_rows, std_rows, norm_factor):
    data_anom = (pred_rows - jnp.mean(pred_rows, axis=1, keepdims=True)) * norm_factor
    innov = obs_rows - pred_rows
    row_weight = 1.0 / (4.0 * std_rows * std_rows)
    scaled = row_weight[:, None] * data_anom
    return (data_anom, innov, row_weight, scaled)


def bit_of(axis, k):
    return (lax.axis_index(axis) // k) % 2


def swap(x, axis, k):
    size = lax.axis_size(axis)
    return lax.ppermute(x, axis, [(i, i ^ k) for i in range(size)])


def axis_bits(axis):
    size = lax.axis_size(axis)
    out, k = [], 1
    while k < size:
        out.append((axis, k))
        k *= 2
    return out


def all_sum(x, steps, halvings, tie):
    for axis, k in steps[:halvings]:
        half = x.shape[0] // 2
        hi = bit_of(axis, k) == 1
        keep = jnp.where(hi, x[half:], x[:half])
        send = jnp.where(hi, x[:half], x[half:])
        x = keep + swap(send, axis, k)
    for axis, k in steps[halvings:]:
        x = x + swap(x, axis, k)
    x, tie = lax.optimization_barrier((x, tie))
    for axis, k in reversed(steps[:halvings]):
        other = swap(x, axis, k)
        hi = bit_of(axis, k) == 1
        x = jnp.where(hi, jnp.concatenate([other, x], 0), jnp.concatenate([x, other], 0))
    return x, tie


def shards(prior_state, pred_data, obs_pert, obs_std, loc_mask, taper_level):
    highest = lax.Precision.HIGHEST
    members = pred_data.shape[1]
    norm_factor = 1.0 / jnp.sqrt(jnp.float32(members - 1))
    data_anom, innov, row_weight, scaled = prepare(pred_data, obs_pert, obs_std, norm_factor)

    stacked = jnp.concatenate(
        [
            jnp.dot(data_anom.T, scaled, precision=highest),
            jnp.dot(scaled.T, innov, precision=highest),
        ],
        0,
    )
    packed = jnp.concatenate([data_anom, innov, row_weight[:, None]], 1)
    order = axis_bits("tile")[:1] + axis_bits("well") + axis_bits("tile")[1:]
    stacked, packed = all_sum(stacked, order, 2, packed)
    gram_matrix, cross_matrix = stacked[:members], stacked[members:]
    own_count = members // lax.axis_size("well")
    own_start = lax.axis_index("well") * own_count
    system = jnp.eye(members, dtype=jnp.float32) + gram_matrix
    head = block_cholesky(system, min(BLOCK, members - 8), highest)

    copies = jnp.broadcast_to(packed[None], (lax.axis_size("tile"),) + packed.shape)
    group = lax.all_to_all(copies, "tile", 0, 0, tiled=False).reshape((-1, packed.shape[1]))
    head, group = lax.optimization_barrier((head, group))
    group_anom, group_innov, group_weight = (
        group[:, :members],
        group[:, members : 2 * members],
        group[:, 2 * members],
    )
    taper_row = loc_mask[0].astype(jnp.float32) * taper_level[0].astype(jnp.float32) / 4.0
    row_taper = jnp.repeat(taper_row, BLOCK)
    tapered = (row_taper * group_weight)[:, None] * group_anom
    both = lax.dot_general(
        jnp.concatenate([group_anom, group_innov], 1),
        tapered,
        (((0,), (0,)), ((), ())),
        precision=highest,
    )
    taper_gram, taper_cross_t = both[:members], both[members:]

    head, taper_gram, taper_cross_t = lax.optimization_barrier((head, taper_gram, taper_cross_t))
    inv11, l21, l22 = head
    factor = (inv11, l21, lower_inverse(l22, highest))
    solved = backward(factor, *forward(factor, cross_matrix, highest), highest)
    space_t = taper_cross_t - lax.dot_general(
        solved, taper_gram, (((0,), (1,)), ((), ())), precision=highest
    )
    for axis, k in reversed(axis_bits("well")):
        half = space_t.shape[0] // 2
        hi = bit_of(axis, k) == 1
        keep = jnp.where(hi, space_t[half:], space_t[:half])
        send = jnp.where(hi, space_t[:half], space_t[half:])
        space_t = keep + swap(send, axis, k)
    state_anom = (prior_state - jnp.mean(prior_state, axis=1, keepdims=True)) * norm_factor
    increment = jnp.einsum("vnc,mn->vmc", state_anom, space_t, precision=highest)
    prior_mine = lax.dynamic_slice_in_dim(prior_state, own_start, own_count, 1)
    return prior_mine + increment


def solution(mesh):
    return jax.shard_map(
        shards,
        mesh=mesh,
        in_specs=(
            P(None, None, "tile"),
            P(("well", "tile"), None),
            P(("well", "tile"), None),
            P(("well", "tile")),
            P("tile", "well"),
            P("tile", "well"),
        ),
        out_specs=P(None, "well", "tile"),
        check_vma=False,
    )
```

```python
import jax
import jax.numpy as jnp
from jax import lax
from jax.sharding import PartitionSpec as P

BLOCK = 128


def lower_inverse(factor, precision):
    eye = jnp.eye(factor.shape[0], dtype=factor.dtype)
    return lax.linalg.triangular_solve(factor, eye, left_side=True, lower=True, transpose_a=False)


def block_cholesky(system, split, precision):
    system = (system + system.T) * 0.5
    a11, a21, a22 = system[:split, :split], system[split:, :split], system[split:, split:]
    l11 = lax.linalg.cholesky(a11, symmetrize_input=False)
    inv11 = lower_inverse(l11, precision)
    l21 = jnp.dot(a21, inv11.T, precision=precision)
    l22 = lax.linalg.cholesky(a22 - jnp.dot(l21, l21.T, precision=precision), symmetrize_input=False)
    return inv11, l21, l22


def forward(parts, right, precision):
    inv11, l21, inv22 = parts
    split = inv11.shape[0]
    y1 = jnp.dot(inv11, right[:split], precision=precision)
    y2 = jnp.dot(inv22, right[split:] - jnp.dot(l21, y1, precision=precision), precision=precision)
    return y1, y2


def backward(parts, y1, y2, precision):
    inv11, l21, inv22 = parts
    x2 = jnp.dot(inv22.T, y2, precision=precision)
    x1 = jnp.dot(inv11.T, y1 - jnp.dot(l21.T, x2, precision=precision), precision=precision)
    return jnp.concatenate([x1, x2], 0)


def prepare(pred_rows, obs_rows, std_rows, norm_factor):
    data_anom = (pred_rows - jnp.mean(pred_rows, axis=1, keepdims=True)) * norm_factor
    innov = obs_rows - pred_rows
    row_weight = 1.0 / (4.0 * std_rows * std_rows)
    scaled = row_weight[:, None] * data_anom
    return (data_anom, innov, row_weight, scaled)


def bit_of(axis, k):
    return (lax.axis_index(axis) // k) % 2


def swap(x, axis, k):
    size = lax.axis_size(axis)
    return lax.ppermute(x, axis, [(i, i ^ k) for i in range(size)])


def axis_bits(axis):
    size = lax.axis_size(axis)
    out, k = [], 1
    while k < size:
        out.append((axis, k))
        k *= 2
    return out


def all_sum(x, steps, halvings, tie):
    for axis, k in steps[:halvings]:
        half = x.shape[0] // 2
        hi = bit_of(axis, k) == 1
        keep = jnp.where(hi, x[half:], x[:half])
        send = jnp.where(hi, x[:half], x[half:])
        x = keep + swap(send, axis, k)
    for axis, k in steps[halvings:]:
        x = x + swap(x, axis, k)
    x, tie = lax.optimization_barrier((x, tie))
    for axis, k in reversed(steps[:halvings]):
        other = swap(x, axis, k)
        hi = bit_of(axis, k) == 1
        x = jnp.where(hi, jnp.concatenate([other, x], 0), jnp.concatenate([x, other], 0))
    return x, tie


def shards(prior_state, pred_data, obs_pert, obs_std, loc_mask, taper_level):
    highest = lax.Precision.HIGHEST
    members = pred_data.shape[1]
    norm_factor = 1.0 / jnp.sqrt(jnp.float32(members - 1))
    data_anom, innov, row_weight, scaled = prepare(pred_data, obs_pert, obs_std, norm_factor)

    stacked = jnp.concatenate(
        [
            jnp.dot(data_anom.T, scaled, precision=highest),
            jnp.dot(scaled.T, innov, precision=highest),
        ],
        0,
    )
    packed = jnp.concatenate([data_anom, innov, row_weight[:, None]], 1)
    order = axis_bits("tile")[:1] + axis_bits("well") + axis_bits("tile")[1:]
    stacked, packed = all_sum(stacked, order, 2, packed)
    gram_matrix, cross_matrix = stacked[:members], stacked[members:]
    own_count = members // lax.axis_size("well")
    own_start = lax.axis_index("well") * own_count
    system = jnp.eye(members, dtype=jnp.float32) + gram_matrix
    head = block_cholesky(system, min(BLOCK, members - 8), highest)

    copies = jnp.broadcast_to(packed[None], (lax.axis_size("tile"),) + packed.shape)
    group = lax.all_to_all(copies, "tile", 0, 0, tiled=False).reshape((-1, packed.shape[1]))
    head, group = lax.optimization_barrier((head, group))
    group_anom, group_innov, group_weight = (
        group[:, :members],
        group[:, members : 2 * members],
        group[:, 2 * members],
    )
    taper_row = loc_mask[0].astype(jnp.float32) * taper_level[0].astype(jnp.float32) / 4.0
    row_taper = jnp.repeat(taper_row, BLOCK)
    tapered = (row_taper * group_weight)[:, None] * group_anom
    both = lax.dot_general(
        jnp.concatenate([group_anom, group_innov], 1),
        tapered,
        (((0,), (0,)), ((), ())),
        precision=highest,
    )
    taper_gram, taper_cross_t = both[:members], both[members:]

    head, taper_gram, taper_cross_t = lax.optimization_barrier((head, taper_gram, taper_cross_t))
    inv11, l21, l22 = head
    factor = (inv11, l21, lower_inverse(l22, highest))
    solved = backward(factor, *forward(factor, cross_matrix, highest), highest)
    space_t = taper_cross_t - lax.dot_general(
        solved, taper_gram, (((0,), (1,)), ((), ())), precision=highest
    )
    wells = lax.axis_size("well")
    blocks = space_t.reshape((wells, space_t.shape[0] // wells, space_t.shape[1]))
    space_t = jnp.sum(lax.all_to_all(blocks, "well", 0, 0, tiled=False), axis=0)
    state_anom = (prior_state - jnp.mean(prior_state, axis=1, keepdims=True)) * norm_factor
    increment = jnp.einsum("vnc,mn->vmc", state_anom, space_t, precision=highest)
    prior_mine = lax.dynamic_slice_in_dim(prior_state, own_start, own_count, 1)
    return prior_mine + increment


def solution(mesh):
    return jax.shard_map(
        shards,
        mesh=mesh,
        in_specs=(
            P(None, None, "tile"),
            P(("well", "tile"), None),
            P(("well", "tile"), None),
            P(("well", "tile")),
            P("tile", "well"),
            P("tile", "well"),
        ),
        out_specs=P(None, "well", "tile"),
        check_vma=False,
    )
```

```python
import jax
import jax.numpy as jnp
from jax import lax
from jax.sharding import PartitionSpec as P

BLOCK = 128


def lower_inverse(factor, precision):
    eye = jnp.eye(factor.shape[0], dtype=factor.dtype)
    return lax.linalg.triangular_solve(factor, eye, left_side=True, lower=True, transpose_a=False)


def block_cholesky(system, split, precision):
    system = (system + system.T) * 0.5
    a11, a21, a22 = system[:split, :split], system[split:, :split], system[split:, split:]
    l11 = lax.linalg.cholesky(a11, symmetrize_input=False)
    inv11 = lower_inverse(l11, precision)
    l21 = jnp.dot(a21, inv11.T, precision=precision)
    l22 = lax.linalg.cholesky(a22 - jnp.dot(l21, l21.T, precision=precision), symmetrize_input=False)
    return inv11, l21, l22


def backward(parts, y1, y2, precision):
    inv11, l21, inv22 = parts
    x2 = jnp.dot(inv22.T, y2, precision=precision)
    x1 = jnp.dot(inv11.T, y1 - jnp.dot(l21.T, x2, precision=precision), precision=precision)
    return jnp.concatenate([x1, x2], 0)


def prepare(pred_rows, obs_rows, std_rows, norm_factor):
    data_anom = (pred_rows - jnp.mean(pred_rows, axis=1, keepdims=True)) * norm_factor
    innov = obs_rows - pred_rows
    row_weight = 1.0 / (4.0 * std_rows * std_rows)
    scaled = row_weight[:, None] * data_anom
    return (data_anom, innov, row_weight, scaled)


def bit_of(axis, k):
    return (lax.axis_index(axis) // k) % 2


def swap(x, axis, k):
    size = lax.axis_size(axis)
    return lax.ppermute(x, axis, [(i, i ^ k) for i in range(size)])


def axis_bits(axis):
    size = lax.axis_size(axis)
    out, k = [], 1
    while k < size:
        out.append((axis, k))
        k *= 2
    return out


def all_sum(x, steps, halvings, tie):
    for axis, k in steps[:halvings]:
        half = x.shape[0] // 2
        hi = bit_of(axis, k) == 1
        keep = jnp.where(hi, x[half:], x[:half])
        send = jnp.where(hi, x[:half], x[half:])
        x = keep + swap(send, axis, k)
    for axis, k in steps[halvings:]:
        x = x + swap(x, axis, k)
    x, tie = lax.optimization_barrier((x, tie))
    for axis, k in reversed(steps[:halvings]):
        other = swap(x, axis, k)
        hi = bit_of(axis, k) == 1
        x = jnp.where(hi, jnp.concatenate([other, x], 0), jnp.concatenate([x, other], 0))
    return x, tie


def shards(prior_state, pred_data, obs_pert, obs_std, loc_mask, taper_level):
    highest = lax.Precision.HIGHEST
    members = pred_data.shape[1]
    norm_factor = 1.0 / jnp.sqrt(jnp.float32(members - 1))
    data_anom, innov, row_weight, scaled = prepare(pred_data, obs_pert, obs_std, norm_factor)

    stacked = jnp.concatenate(
        [
            jnp.dot(data_anom.T, scaled, precision=highest),
            jnp.dot(scaled.T, innov, precision=highest),
        ],
        0,
    )
    packed = jnp.concatenate([data_anom, innov, row_weight[:, None]], 1)
    copies = jnp.broadcast_to(packed[None], (lax.axis_size("tile"),) + packed.shape)
    order = axis_bits("tile")[:1] + axis_bits("well") + axis_bits("tile")[1:]
    stacked, copies = all_sum(stacked, order, 2, copies)
    gram_matrix, cross_matrix = stacked[:members], stacked[members:]
    own_count = members // lax.axis_size("well")
    own_start = lax.axis_index("well") * own_count
    system = jnp.eye(members, dtype=jnp.float32) + gram_matrix
    head = block_cholesky(system, min(BLOCK, members - 8), highest)

    group = lax.all_to_all(copies, "tile", 0, 0, tiled=False).reshape((-1, copies.shape[2]))
    head, group = lax.optimization_barrier((head, group))
    group_anom, group_innov, group_weight = (
        group[:, :members],
        group[:, members : 2 * members],
        group[:, 2 * members],
    )
    taper_row = loc_mask[0].astype(jnp.float32) * taper_level[0].astype(jnp.float32) / 4.0
    row_taper = jnp.repeat(taper_row, BLOCK)
    tapered = (row_taper * group_weight)[:, None] * group_anom
    both = lax.dot_general(
        jnp.concatenate([group_anom, group_innov], 1),
        tapered,
        (((0,), (0,)), ((), ())),
        precision=highest,
    )
    taper_gram, taper_cross_t = both[:members], both[members:]

    inv11, l21, l22 = head
    split = inv11.shape[0]
    y1 = jnp.dot(inv11, cross_matrix[:split], precision=highest)
    rest = cross_matrix[split:] - jnp.dot(l21, y1, precision=highest)
    head, y1, rest, taper_gram, taper_cross_t = lax.optimization_barrier(
        (head, y1, rest, taper_gram, taper_cross_t)
    )
    inv11, l21, l22 = head
    factor = (inv11, l21, lower_inverse(l22, highest))
    solved = backward(factor, y1, jnp.dot(factor[2], rest, precision=highest), highest)
    space_t = taper_cross_t - lax.dot_general(
        solved, taper_gram, (((0,), (1,)), ((), ())), precision=highest
    )
    for axis, k in reversed(axis_bits("well")):
        half = space_t.shape[0] // 2
        hi = bit_of(axis, k) == 1
        keep = jnp.where(hi, space_t[half:], space_t[:half])
        send = jnp.where(hi, space_t[:half], space_t[half:])
        space_t = keep + swap(send, axis, k)
    state_anom = (prior_state - jnp.mean(prior_state, axis=1, keepdims=True)) * norm_factor
    increment = jnp.einsum("vnc,mn->vmc", state_anom, space_t, precision=lax.Precision.HIGH)
    prior_mine = lax.dynamic_slice_in_dim(prior_state, own_start, own_count, 1)
    return prior_mine + increment


def solution(mesh):
    return jax.shard_map(
        shards,
        mesh=mesh,
        in_specs=(
            P(None, None, "tile"),
            P(("well", "tile"), None),
            P(("well", "tile"), None),
            P(("well", "tile")),
            P("tile", "well"),
            P("tile", "well"),
        ),
        out_specs=P(None, "well", "tile"),
        check_vma=False,
    )
```

```python
import jax
import jax.numpy as jnp
from jax import lax
from jax.sharding import PartitionSpec as P

BLOCK = 128


def lower_inverse(factor, precision):
    eye = jnp.eye(factor.shape[0], dtype=factor.dtype)
    return lax.linalg.triangular_solve(factor, eye, left_side=True, lower=True, transpose_a=False)


def block_cholesky(system, split, precision):
    system = (system + system.T) * 0.5
    a11, a21, a22 = system[:split, :split], system[split:, :split], system[split:, split:]
    l11 = lax.linalg.cholesky(a11, symmetrize_input=False)
    inv11 = lower_inverse(l11, precision)
    l21 = jnp.dot(a21, inv11.T, precision=precision)
    l22 = lax.linalg.cholesky(a22 - jnp.dot(l21, l21.T, precision=precision), symmetrize_input=False)
    return inv11, l21, l22


def forward(parts, right, precision):
    inv11, l21, inv22 = parts
    split = inv11.shape[0]
    y1 = jnp.dot(inv11, right[:split], precision=precision)
    y2 = jnp.dot(inv22, right[split:] - jnp.dot(l21, y1, precision=precision), precision=precision)
    return y1, y2


def backward(parts, y1, y2, precision):
    inv11, l21, inv22 = parts
    x2 = jnp.dot(inv22.T, y2, precision=precision)
    x1 = jnp.dot(inv11.T, y1 - jnp.dot(l21.T, x2, precision=precision), precision=precision)
    return jnp.concatenate([x1, x2], 0)


def prepare(pred_rows, obs_rows, std_rows, norm_factor):
    data_anom = (pred_rows - jnp.mean(pred_rows, axis=1, keepdims=True)) * norm_factor
    innov = obs_rows - pred_rows
    row_weight = 1.0 / (4.0 * std_rows * std_rows)
    scaled = row_weight[:, None] * data_anom
    return (data_anom, innov, row_weight, scaled)


def bit_of(axis, k):
    return (lax.axis_index(axis) // k) % 2


def swap(x, axis, k):
    size = lax.axis_size(axis)
    return lax.ppermute(x, axis, [(i, i ^ k) for i in range(size)])


def axis_bits(axis):
    size = lax.axis_size(axis)
    out, k = [], 1
    while k < size:
        out.append((axis, k))
        k *= 2
    return out


def all_sum(x, steps, halvings, tie):
    for axis, k in steps[:halvings]:
        half = x.shape[0] // 2
        hi = bit_of(axis, k) == 1
        keep = jnp.where(hi, x[half:], x[:half])
        send = jnp.where(hi, x[:half], x[half:])
        x = keep + swap(send, axis, k)
    for axis, k in steps[halvings:]:
        x = x + swap(x, axis, k)
    x, tie = lax.optimization_barrier((x, tie))
    for axis, k in reversed(steps[:halvings]):
        other = swap(x, axis, k)
        hi = bit_of(axis, k) == 1
        x = jnp.where(hi, jnp.concatenate([other, x], 0), jnp.concatenate([x, other], 0))
    return x, tie


def shards(prior_state, pred_data, obs_pert, obs_std, loc_mask, taper_level):
    highest = lax.Precision.HIGHEST
    members = pred_data.shape[1]
    norm_factor = 1.0 / jnp.sqrt(jnp.float32(members - 1))
    data_anom, innov, row_weight, scaled = prepare(pred_data, obs_pert, obs_std, norm_factor)

    stacked = jnp.concatenate(
        [
            jnp.dot(data_anom.T, scaled, precision=highest),
            jnp.dot(scaled.T, innov, precision=highest),
        ],
        0,
    )
    packed = jnp.concatenate([data_anom, innov, row_weight[:, None]], 1)
    order = axis_bits("tile")[:1] + axis_bits("well") + axis_bits("tile")[1:]
    stacked, packed = all_sum(stacked, order, 1, packed)
    gram_matrix, cross_matrix = stacked[:members], stacked[members:]
    own_count = members // lax.axis_size("well")
    own_start = lax.axis_index("well") * own_count
    system = jnp.eye(members, dtype=jnp.float32) + gram_matrix
    head = block_cholesky(system, min(BLOCK, members - 8), highest)

    copies = jnp.broadcast_to(packed[None], (lax.axis_size("tile"),) + packed.shape)
    group = lax.all_to_all(copies, "tile", 0, 0, tiled=False).reshape((-1, packed.shape[1]))
    head, group = lax.optimization_barrier((head, group))
    group_anom, group_innov, group_weight = (
        group[:, :members],
        group[:, members : 2 * members],
        group[:, 2 * members],
    )
    taper_row = loc_mask[0].astype(jnp.float32) * taper_level[0].astype(jnp.float32) / 4.0
    row_taper = jnp.repeat(taper_row, BLOCK)
    tapered = (row_taper * group_weight)[:, None] * group_anom
    both = lax.dot_general(
        jnp.concatenate([group_anom, group_innov], 1),
        tapered,
        (((0,), (0,)), ((), ())),
        precision=highest,
    )
    taper_gram, taper_cross_t = both[:members], both[members:]

    head, taper_gram, taper_cross_t = lax.optimization_barrier((head, taper_gram, taper_cross_t))
    inv11, l21, l22 = head
    factor = (inv11, l21, lower_inverse(l22, highest))
    solved = backward(factor, *forward(factor, cross_matrix, highest), highest)
    space_t = taper_cross_t - lax.dot_general(
        solved, taper_gram, (((0,), (1,)), ((), ())), precision=highest
    )
    for axis, k in reversed(axis_bits("well")):
        half = space_t.shape[0] // 2
        hi = bit_of(axis, k) == 1
        keep = jnp.where(hi, space_t[half:], space_t[:half])
        send = jnp.where(hi, space_t[:half], space_t[half:])
        space_t = keep + swap(send, axis, k)
    state_anom = (prior_state - jnp.mean(prior_state, axis=1, keepdims=True)) * norm_factor
    increment = jnp.einsum("vnc,mn->vmc", state_anom, space_t, precision=highest)
    prior_mine = lax.dynamic_slice_in_dim(prior_state, own_start, own_count, 1)
    return prior_mine + increment


def solution(mesh):
    return jax.shard_map(
        shards,
        mesh=mesh,
        in_specs=(
            P(None, None, "tile"),
            P(("well", "tile"), None),
            P(("well", "tile"), None),
            P(("well", "tile")),
            P("tile", "well"),
            P("tile", "well"),
        ),
        out_specs=P(None, "well", "tile"),
        check_vma=False,
    )
```

```python
import jax
import jax.numpy as jnp
from jax import lax
from jax.sharding import PartitionSpec as P

BLOCK = 128


def lower_inverse(factor, precision):
    eye = jnp.eye(factor.shape[0], dtype=factor.dtype)
    return lax.linalg.triangular_solve(factor, eye, left_side=True, lower=True, transpose_a=False)


def block_cholesky(system, split, precision):
    system = (system + system.T) * 0.5
    a11, a21, a22 = system[:split, :split], system[split:, :split], system[split:, split:]
    l11 = lax.linalg.cholesky(a11, symmetrize_input=False)
    inv11 = lower_inverse(l11, precision)
    l21 = jnp.dot(a21, inv11.T, precision=precision)
    l22 = lax.linalg.cholesky(a22 - jnp.dot(l21, l21.T, precision=precision), symmetrize_input=False)
    return inv11, l21, l22


def forward(parts, right, precision):
    inv11, l21, inv22 = parts
    split = inv11.shape[0]
    y1 = jnp.dot(inv11, right[:split], precision=precision)
    y2 = jnp.dot(inv22, right[split:] - jnp.dot(l21, y1, precision=precision), precision=precision)
    return y1, y2


def backward(parts, y1, y2, precision):
    inv11, l21, inv22 = parts
    x2 = jnp.dot(inv22.T, y2, precision=precision)
    x1 = jnp.dot(inv11.T, y1 - jnp.dot(l21.T, x2, precision=precision), precision=precision)
    return jnp.concatenate([x1, x2], 0)


def prepare(pred_rows, obs_rows, std_rows, norm_factor):
    data_anom = (pred_rows - jnp.mean(pred_rows, axis=1, keepdims=True)) * norm_factor
    innov = obs_rows - pred_rows
    row_weight = 1.0 / (4.0 * std_rows * std_rows)
    scaled = row_weight[:, None] * data_anom
    return (data_anom, innov, row_weight, scaled)


def bit_of(axis, k):
    return (lax.axis_index(axis) // k) % 2


def swap(x, axis, k):
    size = lax.axis_size(axis)
    return lax.ppermute(x, axis, [(i, i ^ k) for i in range(size)])


def axis_bits(axis):
    size = lax.axis_size(axis)
    out, k = [], 1
    while k < size:
        out.append((axis, k))
        k *= 2
    return out


def all_sum(first, steps, halvings, tie):
    keep, send = first
    axis, k = steps[0]
    x = keep + swap(send, axis, k)
    for axis, k in steps[1:halvings]:
        half = x.shape[0] // 2
        hi = bit_of(axis, k) == 1
        keep = jnp.where(hi, x[half:], x[:half])
        send = jnp.where(hi, x[:half], x[half:])
        x = keep + swap(send, axis, k)
    for axis, k in steps[halvings:]:
        x = x + swap(x, axis, k)
    x, tie = lax.optimization_barrier((x, tie))
    for axis, k in reversed(steps[:halvings]):
        other = swap(x, axis, k)
        hi = bit_of(axis, k) == 1
        x = jnp.where(hi, jnp.concatenate([other, x], 0), jnp.concatenate([x, other], 0))
    return x, tie


def shards(prior_state, pred_data, obs_pert, obs_std, loc_mask, taper_level):
    highest = lax.Precision.HIGHEST
    members = pred_data.shape[1]
    norm_factor = 1.0 / jnp.sqrt(jnp.float32(members - 1))
    data_anom, innov, row_weight, scaled = prepare(pred_data, obs_pert, obs_std, norm_factor)

    order = axis_bits("tile")[:1] + axis_bits("well") + axis_bits("tile")[1:]
    hi = bit_of(*order[0]) == 1
    halves = [
        jnp.dot(jnp.where(a, scaled, data_anom).T, jnp.where(a, innov, scaled), precision=highest)
        for a in (hi, jnp.logical_not(hi))
    ]
    packed = jnp.concatenate([data_anom, innov, row_weight[:, None]], 1)
    stacked, packed = all_sum(halves, order, 2, packed)
    gram_matrix, cross_matrix = stacked[:members], stacked[members:]
    own_count = members // lax.axis_size("well")
    own_start = lax.axis_index("well") * own_count
    system = jnp.eye(members, dtype=jnp.float32) + gram_matrix
    head = block_cholesky(system, min(BLOCK, members - 8), highest)

    copies = jnp.broadcast_to(packed[None], (lax.axis_size("tile"),) + packed.shape)
    group = lax.all_to_all(copies, "tile", 0, 0, tiled=False).reshape((-1, packed.shape[1]))
    head, group = lax.optimization_barrier((head, group))
    group_anom, group_innov, group_weight = (
        group[:, :members],
        group[:, members : 2 * members],
        group[:, 2 * members],
    )
    taper_row = loc_mask[0].astype(jnp.float32) * taper_level[0].astype(jnp.float32) / 4.0
    row_taper = jnp.repeat(taper_row, BLOCK)
    tapered = (row_taper * group_weight)[:, None] * group_anom
    both = lax.dot_general(
        jnp.concatenate([group_anom, group_innov], 1),
        tapered,
        (((0,), (0,)), ((), ())),
        precision=highest,
    )
    taper_gram, taper_cross_t = both[:members], both[members:]

    head, taper_gram, taper_cross_t = lax.optimization_barrier((head, taper_gram, taper_cross_t))
    inv11, l21, l22 = head
    factor = (inv11, l21, lower_inverse(l22, highest))
    solved = backward(factor, *forward(factor, cross_matrix, highest), highest)
    space_t = taper_cross_t - lax.dot_general(
        solved, taper_gram, (((0,), (1,)), ((), ())), precision=highest
    )
    for axis, k in reversed(axis_bits("well")):
        half = space_t.shape[0] // 2
        hi = bit_of(axis, k) == 1
        keep = jnp.where(hi, space_t[half:], space_t[:half])
        send = jnp.where(hi, space_t[:half], space_t[half:])
        space_t = keep + swap(send, axis, k)
    state_anom = (prior_state - jnp.mean(prior_state, axis=1, keepdims=True)) * norm_factor
    increment = jnp.einsum("vnc,mn->vmc", state_anom, space_t, precision=highest)
    prior_mine = lax.dynamic_slice_in_dim(prior_state, own_start, own_count, 1)
    return prior_mine + increment


def solution(mesh):
    return jax.shard_map(
        shards,
        mesh=mesh,
        in_specs=(
            P(None, None, "tile"),
            P(("well", "tile"), None),
            P(("well", "tile"), None),
            P(("well", "tile")),
            P("tile", "well"),
            P("tile", "well"),
        ),
        out_specs=P(None, "well", "tile"),
        check_vma=False,
    )
```

```python
import jax
import jax.numpy as jnp
from jax import lax
from jax.sharding import PartitionSpec as P

BLOCK = 128


def lower_inverse(factor, precision):
    eye = jnp.eye(factor.shape[0], dtype=factor.dtype)
    return lax.linalg.triangular_solve(factor, eye, left_side=True, lower=True, transpose_a=False)


def block_cholesky(system, split, precision):
    system = (system + system.T) * 0.5
    a11, a21, a22 = system[:split, :split], system[split:, :split], system[split:, split:]
    l11 = lax.linalg.cholesky(a11, symmetrize_input=False)
    inv11 = lower_inverse(l11, precision)
    l21 = jnp.dot(a21, inv11.T, precision=precision)
    l22 = lax.linalg.cholesky(a22 - jnp.dot(l21, l21.T, precision=precision), symmetrize_input=False)
    return inv11, l21, l22


def forward(parts, right, precision):
    inv11, l21, inv22 = parts
    split = inv11.shape[0]
    y1 = jnp.dot(inv11, right[:split], precision=precision)
    y2 = jnp.dot(inv22, right[split:] - jnp.dot(l21, y1, precision=precision), precision=precision)
    return y1, y2


def backward(parts, y1, y2, precision):
    inv11, l21, inv22 = parts
    x2 = jnp.dot(inv22.T, y2, precision=precision)
    x1 = jnp.dot(inv11.T, y1 - jnp.dot(l21.T, x2, precision=precision), precision=precision)
    return jnp.concatenate([x1, x2], 0)


def prepare(pred_rows, obs_rows, std_rows, norm_factor):
    data_anom = (pred_rows - jnp.mean(pred_rows, axis=1, keepdims=True)) * norm_factor
    innov = obs_rows - pred_rows
    row_weight = 1.0 / (4.0 * std_rows * std_rows)
    scaled = row_weight[:, None] * data_anom
    return (data_anom, innov, row_weight, scaled)


def bit_of(axis, k):
    return (lax.axis_index(axis) // k) % 2


def swap(x, axis, k):
    size = lax.axis_size(axis)
    return lax.ppermute(x, axis, [(i, i ^ k) for i in range(size)])


def axis_bits(axis):
    size = lax.axis_size(axis)
    out, k = [], 1
    while k < size:
        out.append((axis, k))
        k *= 2
    return out


def all_sum(x, steps, halvings, tie):
    for axis, k in steps[:halvings]:
        half = x.shape[0] // 2
        hi = bit_of(axis, k) == 1
        keep = jnp.where(hi, x[half:], x[:half])
        send = jnp.where(hi, x[:half], x[half:])
        x = keep + swap(send, axis, k)
    for axis, k in steps[halvings:]:
        x = x + swap(x, axis, k)
    x, tie = lax.optimization_barrier((x, tie))
    for axis, k in reversed(steps[:halvings]):
        other = swap(x, axis, k)
        hi = bit_of(axis, k) == 1
        x = jnp.where(hi, jnp.concatenate([other, x], 0), jnp.concatenate([x, other], 0))
    return x, tie


def well_step(full, split, axis, k):
    half = split.shape[0] // 2
    hi = bit_of(axis, k) == 1
    keep = jnp.where(hi, split[half:], split[:half])
    send = jnp.where(hi, split[:half], split[half:])
    got = swap(jnp.concatenate([full, send], 0), axis, k)
    return full + got[: full.shape[0]], keep + got[full.shape[0]:]


def shards(prior_state, pred_data, obs_pert, obs_std, loc_mask, taper_level):
    highest = lax.Precision.HIGHEST
    members = pred_data.shape[1]
    norm_factor = 1.0 / jnp.sqrt(jnp.float32(members - 1))
    data_anom, innov, row_weight, scaled = prepare(pred_data, obs_pert, obs_std, norm_factor)

    stacked = jnp.concatenate(
        [
            jnp.dot(data_anom.T, scaled, precision=highest),
            jnp.dot(scaled.T, innov, precision=highest),
        ],
        0,
    )
    packed = jnp.concatenate([data_anom, innov, row_weight[:, None]], 1)
    order = axis_bits("tile")[:1] + axis_bits("well") + axis_bits("tile")[1:]
    stacked, packed = all_sum(stacked, order, 2, packed)
    gram_matrix, cross_matrix = stacked[:members], stacked[members:]
    own_count = members // lax.axis_size("well")
    own_start = lax.axis_index("well") * own_count
    system = jnp.eye(members, dtype=jnp.float32) + gram_matrix
    head = block_cholesky(system, min(BLOCK, members - 8), highest)

    copies = jnp.broadcast_to(packed[None], (lax.axis_size("tile"),) + packed.shape)
    group = lax.all_to_all(copies, "tile", 0, 0, tiled=False).reshape((-1, packed.shape[1]))
    head, group = lax.optimization_barrier((head, group))
    group_anom, group_innov, group_weight = (
        group[:, :members],
        group[:, members : 2 * members],
        group[:, 2 * members],
    )
    taper_row = loc_mask[0].astype(jnp.float32) * taper_level[0].astype(jnp.float32) / 4.0
    row_taper = jnp.repeat(taper_row, BLOCK)
    tapered = (row_taper * group_weight)[:, None] * group_anom
    both = lax.dot_general(
        jnp.concatenate([group_anom, group_innov], 1),
        tapered,
        (((0,), (0,)), ((), ())),
        precision=highest,
    )
    taper_gram, taper_cross_t = both[:members], both[members:]

    head, taper_gram, taper_cross_t = lax.optimization_barrier((head, taper_gram, taper_cross_t))
    for axis, k in reversed(axis_bits("well")):
        taper_gram, taper_cross_t = well_step(taper_gram, taper_cross_t, axis, k)
    inv11, l21, l22 = head
    factor = (inv11, l21, lower_inverse(l22, highest))
    solved = backward(factor, *forward(factor, cross_matrix, highest), highest)
    solved_mine = lax.dynamic_slice_in_dim(solved, own_start, own_count, 1)
    space_t = taper_cross_t - lax.dot_general(
        solved_mine, taper_gram, (((0,), (1,)), ((), ())), precision=highest
    )
    state_anom = (prior_state - jnp.mean(prior_state, axis=1, keepdims=True)) * norm_factor
    increment = jnp.einsum("vnc,mn->vmc", state_anom, space_t, precision=highest)
    prior_mine = lax.dynamic_slice_in_dim(prior_state, own_start, own_count, 1)
    return prior_mine + increment


def solution(mesh):
    return jax.shard_map(
        shards,
        mesh=mesh,
        in_specs=(
            P(None, None, "tile"),
            P(("well", "tile"), None),
            P(("well", "tile"), None),
            P(("well", "tile")),
            P("tile", "well"),
            P("tile", "well"),
        ),
        out_specs=P(None, "well", "tile"),
        check_vma=False,
    )
```
